128 devices in a mesh: ord: 16 (over x, y_lo, core), lat: 8 (over z, y_hi).
Axes of the slice: x: 4, y: 4 (y_hi: 2, y_lo: 2; y = y_hi * 2 + y_lo), z: 4, core: 2. Of those that a mesh axis runs over, the one named last changes fastest.
Arguments:
- grad_coef: bfloat16 [768, 768, 256], P(('ord', 'lat')), may hold values from -6 to 6
- legendre: bfloat16 [768, 256, 768], P('ord', 'lat'), may hold values from -0.0078125 to 0.0078125
- quad_weight: float32 [256], P('lat'), may hold values from 0.3 to 1
- slot_order: int32 [768], replicated, may hold values from 0 to 767, as said below
- slot_count: int32 [768], P('ord'), may hold values from 0 to 721, as said below
- conv_input: bfloat16 [256, 128, 1440], P(('lat', 'ord')), may hold values from -6 to 6
- depth_kernel: float32 [128, 25], replicated, may hold values from -1.25 to 1.25
- point_weight: bfloat16 [128, 128], replicated, may hold values from -0.5 to 0.5
Outputs:
- grad_input: bfloat16 [256, 128, 1440], P(('lat', 'ord'))
- grad_point: float32 [128, 128], replicated
- grad_depth: float32 [128, 25], replicated
The draws below stay inside these ranges and needn't reach their ends.
Inputs may be any that keep to these rules, and one draw needn't show every extreme that they name: `slot_order`: a permutation of 0 to 767; slots g*48 to (g+1)*48 - 1 hold the orders of one aligned block of 48 orders, in some order. `slot_count`: 721 minus the slot's order in slot_order, or 0 where that is negative.
All inputs are finite; a program needn't handle non-finite values.
Results may differ from the reference program's by a relative error of at most 0.0068.
Values may be sent and summed in bfloat16 or wider, within the bound.
No kernel may reach another device: no remote copies, remote signals or barrier semaphores. Data moves between devices by JAX's collectives and lax.ppermute only.
A program may use at most 192 MiB of HBM per device.

```python
import math
import jax
import jax.numpy as jnp
from jax import lax

C = 128
NLON = 1440
LMAX = 720
MSLOTS = 768
DEG = 768
NLAT = 256
SLOT_GROUP = 48


def order_layout(key):
    base_key = jax.random.fold_in(key, 7)
    group_key, inner_key = jax.random.split(base_key)
    groups = MSLOTS // SLOT_GROUP
    group_perm = jax.random.permutation(group_key, groups).astype(jnp.int32)
    inner_perm = jax.vmap(lambda sub_key: jax.random.permutation(sub_key, SLOT_GROUP))(jax.random.split(inner_key, groups))
    inner_perm = inner_perm.astype(jnp.int32)
    return (group_perm[:, None] * SLOT_GROUP + inner_perm).reshape(MSLOTS)


def draw_slot_order(key, part):
    return order_layout(key)


def draw_slot_count(key, part):
    return jnp.maximum(LMAX + 1 - order_layout(key), 0).astype(jnp.int32)


def steps_of(stream_key, dims, shards, low, largest):
    gain = 1.0
    for dim, blocks in shards:
        heights = jax.random.uniform(jax.random.fold_in(jax.random.fold_in(stream_key, 6), dim), (blocks,), jnp.float32, low / len(shards), largest / len(shards))
        gain = gain * jnp.repeat(jnp.exp(heights), dims[dim] // blocks).reshape((-1,) + (1,) * (len(dims) - 1 - dim))
    return gain


def scatter_about(key, dims, width, most, shards=(), kind=jnp.bfloat16):
    loudness = steps_of(key, dims, shards, -0.22, 0.18) if shards else 1.0
    drawn = jax.random.normal(key, dims, jnp.float32) * width * loudness
    return jnp.minimum(jnp.maximum(drawn, -most), most).astype(kind)


def setup_inputs(seed: int = 0) -> dict:
    key_of = jax.random.split(jax.random.key(seed), 9)
    grad_coef = scatter_about(key_of[0], (MSLOTS, DEG, 2 * C), 1.0, 6.0, ((0, 128),))
    legendre = scatter_about(key_of[1], (MSLOTS, NLAT, DEG), (1.0 / DEG), 0.0078125, ((0, 16), (1, 8)))
    quad_weight = jnp.clip(0.3 + 0.7 * jax.random.uniform(key_of[2], (NLAT,), jnp.float32) ** steps_of(key_of[2], (NLAT,), ((0, 8),), -0.2, 0.2), 0.3, 1.0)
    slot_order = draw_slot_order(jax.random.fold_in(key_of[8], 71), 0)
    slot_count = draw_slot_count(jax.random.fold_in(key_of[8], 71), 0)
    conv_input = scatter_about(key_of[5], (NLAT, C, NLON), 1.0, 6.0, ((0, 128),))
    depth_kernel = scatter_about(key_of[6], (C, 25), 25 ** -0.5, 1.25, (), jnp.float32)
    point_weight = scatter_about(key_of[7], (C, C), C ** -0.5, 0.5)
    return dict(grad_coef=grad_coef, legendre=legendre, quad_weight=quad_weight, slot_order=slot_order, slot_count=slot_count, conv_input=conv_input, depth_kernel=depth_kernel, point_weight=point_weight)


def make_table(orders, length):
    lon_ids = jnp.arange(length, dtype=jnp.int32)
    residue = orders[:, None] * lon_ids[None, :] % length
    angles = residue.astype(jnp.float32) * (2.0 * math.pi / length)
    factor = jnp.where((orders == 0) | (2 * orders == length), 1.0, 2.0).astype(jnp.float32)[:, None]
    return jnp.stack([factor * jnp.cos(angles), -factor * jnp.sin(angles)], axis=1).astype(jnp.bfloat16)

def reference(grad_coef, legendre, quad_weight, slot_order, slot_count, conv_input, depth_kernel, point_weight):
    degree_ids = jnp.arange(DEG, dtype=jnp.int32)
    is_valid = (degree_ids[None, :] < slot_count[:, None]).astype(jnp.bfloat16)
    masked = grad_coef * is_valid[:, :, None]

    def one_slot(operands):
        table_slot, coef_slot = operands
        return jnp.dot(table_slot, coef_slot, preferred_element_type=jnp.float32)
    spectral = (lax.map(one_slot, (legendre, masked)) * quad_weight[None, :, None]).astype(jnp.bfloat16)
    dft_table = make_table(slot_order, NLON).reshape(MSLOTS * 2, NLON)
    flat_spec = spectral.reshape(MSLOTS, NLAT, C, 2).transpose(1, 2, 0, 3).reshape(NLAT * C, MSLOTS * 2)
    grad_grid = jnp.dot(flat_spec, dft_table, preferred_element_type=jnp.float32)
    grad_grid = grad_grid.reshape(NLAT, C, NLON).astype(jnp.bfloat16)
    padded_x = jnp.pad(conv_input, ((2, 2), (0, 0), (0, 0))).astype(jnp.float32)
    hidden = jnp.zeros((NLAT, C, NLON), jnp.float32)
    for tap_row in range(5):
        for tap_col in range(5):
            weight_tap = depth_kernel[:, 5 * tap_row + tap_col][None, :, None]
            hidden = hidden + weight_tap * jnp.roll(padded_x[tap_row:tap_row + NLAT], 2 - tap_col, axis=2)
    hidden = hidden.astype(jnp.bfloat16)
    grid_wide = grad_grid.astype(jnp.float32)
    grad_hidden = jnp.einsum('cd,rdf->rcf', point_weight.astype(jnp.float32), grid_wide).astype(jnp.bfloat16)
    grad_scale = 1.0 / math.sqrt(NLAT * NLON)
    grad_point = jnp.einsum('rcf,rdf->cd', hidden.astype(jnp.float32), grid_wide) * grad_scale
    hidden_wide = grad_hidden.astype(jnp.float32)
    padded_grad = jnp.pad(hidden_wide, ((2, 2), (0, 0), (0, 0)))
    grad_input = jnp.zeros((NLAT, C, NLON), jnp.float32)
    grad_terms = []
    for tap_row in range(5):
        for tap_col in range(5):
            weight_tap = depth_kernel[:, 5 * tap_row + tap_col][None, :, None]
            grad_input = grad_input + weight_tap * jnp.roll(padded_grad[4 - tap_row:4 - tap_row + NLAT], tap_col - 2, axis=2)
            shifted_x = jnp.roll(padded_x[tap_row:tap_row + NLAT], 2 - tap_col, axis=2)
            grad_terms.append(lax.optimization_barrier(jnp.sum(hidden_wide * shifted_x, axis=(0, 2))))
    grad_depth = jnp.stack(grad_terms, axis=1) * grad_scale
    return (grad_input.astype(jnp.bfloat16), grad_point, grad_depth)
```

```python
import math

import jax
import jax.numpy as jnp
from jax import lax
from jax.sharding import PartitionSpec as P

MESH_AXES = ("ord", "lat")


def device_of_block(k):
    n_ord, n_lat = lax.axis_size("ord"), lax.axis_size("lat")
    l, o = divmod(k, n_ord)
    return o * n_lat + l


def with_rims(field, width=2):
    count = lax.axis_size("ord") * lax.axis_size("lat")
    down_pairs = [(device_of_block(k), device_of_block(k + 1)) for k in range(count - 1)]
    up_pairs = [(device_of_block(k + 1), device_of_block(k)) for k in range(count - 1)]
    upper = lax.ppermute(field[field.shape[0] - width :], MESH_AXES, down_pairs)
    lower = lax.ppermute(field[:width], MESH_AXES, up_pairs)
    return jnp.concatenate([upper, field, lower], axis=0)


def make_table(orders, length):
    lon_ids = jnp.arange(length, dtype=jnp.int32)
    residue = orders[:, None] * lon_ids[None, :] % length
    angles = residue.astype(jnp.float32) * (2.0 * math.pi / length)
    factor = jnp.where((orders == 0) | (2 * orders == length), 1.0, 2.0).astype(jnp.float32)[
        :, None
    ]
    return jnp.stack([factor * jnp.cos(angles), -factor * jnp.sin(angles)], axis=1).astype(
        jnp.bfloat16
    )


def inverse_lon(spec_rows, dft_table):
    slots_here, rows_here, doubled = spec_rows.shape
    paired = spec_rows.reshape(slots_here, rows_here, doubled // 2, 2)
    return jnp.einsum("srcp,spf->rcf", paired, dft_table, preferred_element_type=jnp.float32)


def shards(
    grad_coef, legendre, quad_weight, slot_order, slot_count, conv_input, depth_kernel, point_weight
):
    n_ord = lax.axis_size("ord")
    n_lat = lax.axis_size("lat")
    own_slots, degrees, doubled = grad_coef.shape
    row_count, channels, longitudes = conv_input.shape
    lat_index = lax.axis_index("lat")

    x_wide = with_rims(conv_input).astype(jnp.float32)

    leg_rows = lax.all_to_all(legendre, "lat", 0, 1, tiled=True)
    weights = lax.all_gather(quad_weight, "lat", axis=0, tiled=True)
    counts = lax.dynamic_slice_in_dim(slot_count, lat_index * own_slots, own_slots)
    is_valid = jnp.arange(degrees, dtype=jnp.int32)[None, :] < counts[:, None]
    masked = grad_coef * is_valid[:, :, None].astype(grad_coef.dtype)
    summed = jnp.einsum("slj,sjk->slk", leg_rows, masked, preferred_element_type=jnp.float32)
    spectral = (summed * weights[None, :, None]).astype(jnp.bfloat16)
    by_device = spectral.reshape(own_slots, n_lat, n_ord, row_count, doubled)
    by_device = by_device.transpose(0, 2, 1, 3, 4).reshape(own_slots, -1, doubled)
    own_rows = lax.all_to_all(by_device, MESH_AXES, 1, 0, tiled=True)

    grad_grid = inverse_lon(own_rows, make_table(slot_order, longitudes))
    grad_grid = grad_grid.astype(jnp.bfloat16)

    hidden = jnp.zeros((row_count, channels, longitudes), jnp.float32)
    for tap_row in range(5):
        for tap_col in range(5):
            weight_tap = depth_kernel[:, 5 * tap_row + tap_col][None, :, None]
            hidden = hidden + weight_tap * jnp.roll(
                x_wide[tap_row : tap_row + row_count], 2 - tap_col, axis=2
            )
    hidden = hidden.astype(jnp.bfloat16)
    grad_hidden = jnp.einsum(
        "cd,rdf->rcf", point_weight, grad_grid, preferred_element_type=jnp.float32
    ).astype(jnp.bfloat16)
    point_part = jnp.einsum("rcf,rdf->cd", hidden, grad_grid, preferred_element_type=jnp.float32)
    hidden_wide = grad_hidden.astype(jnp.float32)
    depth_terms = []
    for tap_row in range(5):
        for tap_col in range(5):
            shifted_x = jnp.roll(x_wide[tap_row : tap_row + row_count], 2 - tap_col, axis=2)
            depth_terms.append(jnp.sum(hidden_wide * shifted_x, axis=(0, 2)))
    depth_part = jnp.stack(depth_terms, axis=1)
    sums = lax.psum(jnp.concatenate([point_part, depth_part], axis=1), MESH_AXES)

    padded_grad = with_rims(grad_hidden).astype(jnp.float32)
    grad_input = jnp.zeros((row_count, channels, longitudes), jnp.float32)
    for tap_row in range(5):
        for tap_col in range(5):
            weight_tap = depth_kernel[:, 5 * tap_row + tap_col][None, :, None]
            grad_input = grad_input + weight_tap * jnp.roll(
                padded_grad[4 - tap_row : 4 - tap_row + row_count], tap_col - 2, axis=2
            )
    total_rows = row_count * n_ord * n_lat
    grad_scale = 1.0 / math.sqrt(total_rows * longitudes)
    sums = sums * grad_scale
    return (grad_input.astype(jnp.bfloat16), sums[:, :channels], sums[:, channels:])


def solution(mesh):
    return jax.shard_map(
        shards,
        mesh=mesh,
        in_specs=(
            P(("ord", "lat"), None, None),
            P("ord", "lat", None),
            P("lat"),
            P(),
            P("ord"),
            P(("lat", "ord"), None, None),
            P(),
            P(),
        ),
        out_specs=(P(("lat", "ord"), None, None), P(), P()),
        check_vma=False,
    )
```

```python
import math

import jax
import jax.numpy as jnp
from jax import lax
from jax.sharding import PartitionSpec as P

MESH_AXES = ("ord", "lat")


def device_of_block(k):
    n_ord, n_lat = lax.axis_size("ord"), lax.axis_size("lat")
    l, o = divmod(k, n_ord)
    return o * n_lat + l


def with_rims(field, width=2):
    count = lax.axis_size("ord") * lax.axis_size("lat")
    down_pairs = [(device_of_block(k), device_of_block(k + 1)) for k in range(count - 1)]
    up_pairs = [(device_of_block(k + 1), device_of_block(k)) for k in range(count - 1)]
    upper = lax.ppermute(field[field.shape[0] - width :], MESH_AXES, down_pairs)
    lower = lax.ppermute(field[:width], MESH_AXES, up_pairs)
    return jnp.concatenate([upper, field, lower], axis=0)


def butterfly_sum(value):
    count = lax.axis_size("ord") * lax.axis_size("lat")
    bits = count.bit_length() - 1
    order = sorted(range(bits), key=lambda b: (b != 3, b))
    for bit in order:
        pairs = [(d, d ^ (1 << bit)) for d in range(count)]
        value = value + lax.ppermute(value, MESH_AXES, pairs)
    return value


def make_table(orders, length):
    lon_ids = jnp.arange(length, dtype=jnp.int32)
    residue = orders[:, None] * lon_ids[None, :] % length
    angles = residue.astype(jnp.float32) * (2.0 * math.pi / length)
    factor = jnp.where((orders == 0) | (2 * orders == length), 1.0, 2.0).astype(jnp.float32)[
        :, None
    ]
    parts = [factor * jnp.cos(angles), -factor * jnp.sin(angles)]
    return jnp.concatenate(parts, axis=1).astype(jnp.bfloat16)


def shards(
    grad_coef, legendre, quad_weight, slot_order, slot_count, conv_input, depth_kernel, point_weight
):
    n_ord = lax.axis_size("ord")
    n_lat = lax.axis_size("lat")
    own_slots, degrees, doubled = grad_coef.shape
    row_count, channels, longitudes = conv_input.shape
    lat_index = lax.axis_index("lat")

    x_wide = with_rims(conv_input).astype(jnp.float32)

    leg_rows = lax.all_to_all(legendre, "lat", 0, 1, tiled=True)
    spread = jnp.broadcast_to(quad_weight[None], (n_lat,) + quad_weight.shape)
    weights = lax.all_to_all(spread, "lat", 0, 0, tiled=True).reshape(-1)
    counts = lax.dynamic_slice_in_dim(slot_count, lat_index * own_slots, own_slots)
    is_valid = jnp.arange(degrees, dtype=jnp.int32)[None, :] < counts[:, None]
    masked = grad_coef * is_valid[:, :, None].astype(grad_coef.dtype)
    source = jnp.arange(doubled, dtype=jnp.int32)
    target = (source % 2) * channels + source // 2
    permute = (target[:, None] == source[None, :]).astype(grad_coef.dtype)
    masked = jnp.einsum("sjk,kt->sjt", masked, permute, preferred_element_type=jnp.float32)
    masked = masked.astype(grad_coef.dtype)
    summed = jnp.einsum("slj,sjk->slk", leg_rows, masked, preferred_element_type=jnp.float32)
    spectral = (summed * weights[None, :, None]).astype(jnp.bfloat16)
    by_device = spectral.reshape(own_slots, n_lat, n_ord, row_count * doubled)
    by_device = by_device.transpose(0, 2, 1, 3).reshape(own_slots, n_ord * n_lat, -1)
    own_rows = lax.all_to_all(by_device, MESH_AXES, 1, 0, tiled=True)
    own_rows = own_rows.reshape(-1, row_count * doubled)

    table = make_table(slot_order, longitudes)
    both = jnp.einsum("sn,sq->nq", own_rows, table, preferred_element_type=jnp.float32)
    both = both.reshape(row_count, 2, channels, 2 * longitudes)
    grad_grid = both[:, 0, :, :longitudes] + both[:, 1, :, longitudes:]
    grad_grid = grad_grid.reshape(row_count, channels, longitudes).astype(jnp.bfloat16)

    hidden = jnp.zeros((row_count, channels, longitudes), jnp.float32)
    for tap_row in range(5):
        for tap_col in range(5):
            weight_tap = depth_kernel[:, 5 * tap_row + tap_col][None, :, None]
            hidden = hidden + weight_tap * jnp.roll(
                x_wide[tap_row : tap_row + row_count], 2 - tap_col, axis=2
            )
    hidden = hidden.astype(jnp.bfloat16)
    grad_hidden = jnp.einsum(
        "cd,rdf->rcf", point_weight, grad_grid, preferred_element_type=jnp.float32
    ).astype(jnp.bfloat16)
    point_part = jnp.einsum("rcf,rdf->cd", hidden, grad_grid, preferred_element_type=jnp.float32)
    hidden_wide = grad_hidden.astype(jnp.float32)
    depth_terms = []
    for tap_row in range(5):
        for tap_col in range(5):
            shifted_x = jnp.roll(x_wide[tap_row : tap_row + row_count], 2 - tap_col, axis=2)
            depth_terms.append(jnp.sum(hidden_wide * shifted_x, axis=(0, 2)))
    depth_part = jnp.stack(depth_terms, axis=1)
    sums = butterfly_sum(jnp.concatenate([point_part, depth_part], axis=1))

    padded_grad = with_rims(grad_hidden).astype(jnp.float32)
    grad_input = jnp.zeros((row_count, channels, longitudes), jnp.float32)
    for tap_row in range(5):
        for tap_col in range(5):
            weight_tap = depth_kernel[:, 5 * tap_row + tap_col][None, :, None]
            grad_input = grad_input + weight_tap * jnp.roll(
                padded_grad[4 - tap_row : 4 - tap_row + row_count], tap_col - 2, axis=2
            )
    total_rows = row_count * n_ord * n_lat
    grad_scale = 1.0 / math.sqrt(total_rows * longitudes)
    sums = sums * grad_scale
    return (grad_input.astype(jnp.bfloat16), sums[:, :channels], sums[:, channels:])


def solution(mesh):
    return jax.shard_map(
        shards,
        mesh=mesh,
        in_specs=(
            P(("ord", "lat"), None, None),
            P("ord", "lat", None),
            P("lat"),
            P(),
            P("ord"),
            P(("lat", "ord"), None, None),
            P(),
            P(),
        ),
        out_specs=(P(("lat", "ord"), None, None), P(), P()),
        check_vma=False,
    )
```

```python
import math

import jax
import jax.numpy as jnp
from jax import lax
from jax.sharding import PartitionSpec as P


MESH_AXES = ("ord", "lat")


def device_of_block(k):
    n_ord, n_lat = lax.axis_size("ord"), lax.axis_size("lat")
    l, o = divmod(k, n_ord)
    return o * n_lat + l


def with_rims(field, width=2):
    count = lax.axis_size("ord") * lax.axis_size("lat")
    down_pairs = [(device_of_block(k), device_of_block(k + 1)) for k in range(count - 1)]
    up_pairs = [(device_of_block(k + 1), device_of_block(k)) for k in range(count - 1)]
    upper = lax.ppermute(field[field.shape[0] - width :], MESH_AXES, down_pairs)
    lower = lax.ppermute(field[:width], MESH_AXES, up_pairs)
    return jnp.concatenate([upper, field, lower], axis=0)


def butterfly_sum(value, carry, steps):
    count = lax.axis_size("ord") * lax.axis_size("lat")
    bits = count.bit_length() - 1
    order = sorted(range(bits), key=lambda b: (b != 3, b))
    for round_index, bit in enumerate(order):
        pairs = [(d, d ^ (1 << bit)) for d in range(count)]
        received = lax.ppermute(value, MESH_AXES, pairs)
        if round_index < len(steps):
            carry = steps[round_index](carry)
        value, carry = lax.optimization_barrier((value + received, carry))
    for step in steps[len(order):]:
        carry = step(carry)
    return value, carry


def make_table(orders, length):
    lon_ids = jnp.arange(length, dtype=jnp.int32)
    residue = orders[:, None] * lon_ids[None, :] % length
    angles = residue.astype(jnp.float32) * (2.0 * math.pi / length)
    factor = jnp.where((orders == 0) | (2 * orders == length), 1.0, 2.0).astype(jnp.float32)[
        :, None
    ]
    parts = [factor * jnp.cos(angles), -factor * jnp.sin(angles)]
    return jnp.concatenate(parts, axis=1).astype(jnp.bfloat16)


def layer(
    grad_coef, legendre, quad_weight, slot_order, slot_count, conv_input, depth_kernel, point_weight
):
    n_ord = lax.axis_size("ord")
    n_lat = lax.axis_size("lat")
    own_slots, degrees, doubled = grad_coef.shape
    row_count, channels, longitudes = conv_input.shape
    lat_index = lax.axis_index("lat")

    x_wide = with_rims(conv_input).astype(jnp.float32)

    leg_rows = lax.all_to_all(legendre, "lat", 0, 1, tiled=True)
    spread = jnp.broadcast_to(quad_weight[None], (n_lat,) + quad_weight.shape)
    weights = lax.all_to_all(spread, "lat", 0, 0, tiled=True).reshape(-1)
    counts = lax.dynamic_slice_in_dim(slot_count, lat_index * own_slots, own_slots)
    is_valid = jnp.arange(degrees, dtype=jnp.int32)[None, :] < counts[:, None]
    masked = grad_coef * is_valid[:, :, None].astype(grad_coef.dtype)
    source = jnp.arange(doubled, dtype=jnp.int32)
    target = (source % 2) * channels + source // 2
    permute = (target[:, None] == source[None, :]).astype(grad_coef.dtype)
    masked = jnp.einsum("sjk,kt->sjt", masked, permute, preferred_element_type=jnp.float32)
    masked = masked.astype(grad_coef.dtype)
    summed = jnp.einsum("slj,sjk->slk", leg_rows, masked, preferred_element_type=jnp.float32)
    spectral = (summed * weights[None, :, None]).astype(jnp.bfloat16)
    by_device = spectral.reshape(own_slots, n_lat, n_ord, row_count * doubled)
    by_device = by_device.transpose(0, 2, 1, 3).reshape(own_slots, n_ord * n_lat, -1)
    own_rows = lax.all_to_all(by_device, MESH_AXES, 1, 0, tiled=True)
    own_rows = own_rows.reshape(-1, row_count * doubled)

    table = make_table(slot_order, longitudes)
    both = jnp.einsum("sn,sq->nq", own_rows, table, preferred_element_type=jnp.float32)
    both = both.reshape(row_count, 2, channels, 2 * longitudes)
    grad_grid = both[:, 0, :, :longitudes] + both[:, 1, :, longitudes:]
    grad_grid = grad_grid.reshape(row_count, channels, longitudes).astype(jnp.bfloat16)

    hidden = jnp.zeros((row_count, channels, longitudes), jnp.float32)
    for tap_row in range(5):
        for tap_col in range(5):
            weight_tap = depth_kernel[:, 5 * tap_row + tap_col][None, :, None]
            hidden = hidden + weight_tap * jnp.roll(
                x_wide[tap_row : tap_row + row_count], 2 - tap_col, axis=2
            )
    hidden = hidden.astype(jnp.bfloat16)
    grad_hidden = jnp.einsum(
        "cd,rdf->rcf", point_weight, grad_grid, preferred_element_type=jnp.float32
    ).astype(jnp.bfloat16)
    point_part = jnp.einsum("rcf,rdf->cd", hidden, grad_grid, preferred_element_type=jnp.float32)
    hidden_wide = grad_hidden.astype(jnp.float32)
    depth_terms = []
    for tap_row in range(5):
        for tap_col in range(5):
            shifted_x = jnp.roll(x_wide[tap_row : tap_row + row_count], 2 - tap_col, axis=2)
            depth_terms.append(jnp.sum(hidden_wide * shifted_x, axis=(0, 2)))
    depth_part = jnp.stack(depth_terms, axis=1)
    padded_grad = with_rims(grad_hidden).astype(jnp.float32)
    taps = [(tap_row, tap_col) for tap_row in range(5) for tap_col in range(5)]
    rounds = (n_ord * n_lat).bit_length() - 1
    groups = [taps[i * len(taps) // rounds : (i + 1) * len(taps) // rounds] for i in range(rounds)]

    def tap_group(group):
        def step(grad_input):
            for tap_row, tap_col in group:
                weight_tap = depth_kernel[:, 5 * tap_row + tap_col][None, :, None]
                grad_input = grad_input + weight_tap * jnp.roll(
                    padded_grad[4 - tap_row : 4 - tap_row + row_count], tap_col - 2, axis=2
                )
            return grad_input

        return step

    grad_input = jnp.zeros((row_count, channels, longitudes), jnp.float32)
    sums, grad_input = butterfly_sum(
        jnp.concatenate([point_part, depth_part], axis=1),
        grad_input,
        [tap_group(group) for group in groups],
    )
    total_rows = row_count * n_ord * n_lat
    grad_scale = 1.0 / math.sqrt(total_rows * longitudes)
    sums = sums * grad_scale
    return (grad_input.astype(jnp.bfloat16), sums[:, :channels], sums[:, channels:])


def solution(mesh):
    return jax.shard_map(
        layer,
        mesh=mesh,
        in_specs=(
            P(("ord", "lat"), None, None),
            P("ord", "lat", None),
            P("lat"),
            P(),
            P("ord"),
            P(("lat", "ord"), None, None),
            P(),
            P(),
        ),
        out_specs=(P(("lat", "ord"), None, None), P(), P()),
        check_vma=False,
    )
```

```python
import math

import jax
import jax.numpy as jnp
from jax import lax
from jax.sharding import PartitionSpec as P


MESH_AXES = ("ord", "lat")


def device_of_block(k):
    n_ord, n_lat = lax.axis_size("ord"), lax.axis_size("lat")
    l, o = divmod(k, n_ord)
    return o * n_lat + l


def with_rims(field, width=2):
    count = lax.axis_size("ord") * lax.axis_size("lat")
    down_pairs = [(device_of_block(k), device_of_block(k + 1)) for k in range(count - 1)]
    up_pairs = [(device_of_block(k + 1), device_of_block(k)) for k in range(count - 1)]
    upper = lax.ppermute(field[field.shape[0] - width :], MESH_AXES, down_pairs)
    lower = lax.ppermute(field[:width], MESH_AXES, up_pairs)
    return jnp.concatenate([upper, field, lower], axis=0)


def butterfly_sum(value, carry, steps):
    count = lax.axis_size("ord") * lax.axis_size("lat")
    bits = count.bit_length() - 1
    order = sorted(range(bits), key=lambda b: (b != 3, b))
    for round_index, bit in enumerate(order):
        pairs = [(d, d ^ (1 << bit)) for d in range(count)]
        received = lax.ppermute(value, MESH_AXES, pairs)
        if round_index < len(steps):
            carry = steps[round_index](carry)
        value, carry = lax.optimization_barrier((value + received, carry))
    for step in steps[len(order):]:
        carry = step(carry)
    return value, carry


def wrap_longitudes(field, width):
    return jnp.concatenate([field[:, -width:], field, field[:, :width]], axis=1)


def make_table(orders, length):
    lon_ids = jnp.arange(length, dtype=jnp.int32)
    residue = orders[:, None] * lon_ids[None, :] % length
    angles = residue.astype(jnp.float32) * (2.0 * math.pi / length)
    factor = jnp.where((orders == 0) | (2 * orders == length), 1.0, 2.0).astype(jnp.float32)[
        :, None
    ]
    parts = [factor * jnp.cos(angles), -factor * jnp.sin(angles)]
    return jnp.concatenate(parts, axis=1).astype(jnp.bfloat16)


def layer(
    grad_coef, legendre, quad_weight, slot_order, slot_count, conv_input, depth_kernel, point_weight
):
    n_ord = lax.axis_size("ord")
    n_lat = lax.axis_size("lat")
    own_slots, degrees, doubled = grad_coef.shape
    row_count, channels, longitudes = conv_input.shape
    lat_index = lax.axis_index("lat")

    x_rows = with_rims(conv_input.transpose(0, 2, 1))
    x_pad = wrap_longitudes(x_rows, 2).astype(jnp.float32)

    leg_rows = lax.all_to_all(legendre, "lat", 0, 1, tiled=True)
    spread = jnp.broadcast_to(quad_weight[None], (n_lat,) + quad_weight.shape)
    weights = lax.all_to_all(spread, "lat", 0, 0, tiled=True).reshape(-1)
    counts = lax.dynamic_slice_in_dim(slot_count, lat_index * own_slots, own_slots)
    is_valid = jnp.arange(degrees, dtype=jnp.int32)[None, :] < counts[:, None]
    masked = grad_coef * is_valid[:, :, None].astype(grad_coef.dtype)
    source = jnp.arange(doubled, dtype=jnp.int32)
    target = (source % 2) * channels + source // 2
    permute = (target[:, None] == source[None, :]).astype(grad_coef.dtype)
    masked = jnp.einsum("sjk,kt->sjt", masked, permute, preferred_element_type=jnp.float32)
    masked = masked.astype(grad_coef.dtype)
    summed = jnp.einsum("slj,sjk->slk", leg_rows, masked, preferred_element_type=jnp.float32)
    spectral = (summed * weights[None, :, None]).astype(jnp.bfloat16)
    by_device = spectral.reshape(own_slots, n_lat, n_ord, row_count * doubled)
    by_device = by_device.transpose(0, 2, 1, 3).reshape(own_slots, n_ord * n_lat, -1)
    own_rows = lax.all_to_all(by_device, MESH_AXES, 1, 0, tiled=True)
    own_rows = own_rows.reshape(-1, row_count * doubled)

    table = make_table(slot_order, longitudes)
    per_row = own_rows.reshape(-1, row_count, doubled)
    grid_rows = []
    for row in range(row_count):
        both = jnp.einsum("sq,sn->qn", table, per_row[:, row], preferred_element_type=jnp.float32)
        grid_rows.append(both[:longitudes, :channels] + both[longitudes:, channels:])
    grad_grid = jnp.stack(grid_rows).astype(jnp.bfloat16)

    hidden = jnp.zeros((row_count, longitudes, channels), jnp.float32)
    for tap_row in range(5):
        for tap_col in range(5):
            weight_tap = depth_kernel[:, 5 * tap_row + tap_col]
            hidden = hidden + weight_tap * x_pad[
                tap_row : tap_row + row_count, tap_col : tap_col + longitudes
            ]
    hidden = hidden.astype(jnp.bfloat16)
    grad_hidden = jnp.einsum(
        "rqd,cd->rqc", grad_grid, point_weight, preferred_element_type=jnp.float32
    ).astype(jnp.bfloat16)
    point_part = jnp.einsum("rqc,rqd->cd", hidden, grad_grid, preferred_element_type=jnp.float32)
    hidden_wide = grad_hidden.astype(jnp.float32)
    depth_terms = []
    for tap_row in range(5):
        for tap_col in range(5):
            shifted_x = x_pad[tap_row : tap_row + row_count, tap_col : tap_col + longitudes]
            depth_terms.append(jnp.sum(hidden_wide * shifted_x, axis=(0, 1)))
    depth_part = jnp.stack(depth_terms, axis=1)
    grad_pad = wrap_longitudes(with_rims(grad_hidden), 2).astype(jnp.float32)
    taps = [(tap_row, tap_col) for tap_row in range(5) for tap_col in range(5)]
    rounds = (n_ord * n_lat).bit_length() - 1
    groups = [taps[i * len(taps) // rounds : (i + 1) * len(taps) // rounds] for i in range(rounds)]

    def tap_group(group):
        def step(grad_input):
            for tap_row, tap_col in group:
                weight_tap = depth_kernel[:, 5 * tap_row + tap_col]
                grad_input = grad_input + weight_tap * grad_pad[
                    4 - tap_row : 4 - tap_row + row_count, 4 - tap_col : 4 - tap_col + longitudes
                ]
            return grad_input

        return step

    grad_input = jnp.zeros((row_count, longitudes, channels), jnp.float32)
    sums, grad_input = butterfly_sum(
        jnp.concatenate([point_part, depth_part], axis=1),
        grad_input,
        [tap_group(group) for group in groups],
    )
    grad_input = grad_input.astype(jnp.bfloat16).transpose(0, 2, 1)
    total_rows = row_count * n_ord * n_lat
    grad_scale = 1.0 / math.sqrt(total_rows * longitudes)
    sums = sums * grad_scale
    return (grad_input, sums[:, :channels], sums[:, channels:])


def solution(mesh):
    return jax.shard_map(
        layer,
        mesh=mesh,
        in_specs=(
            P(("ord", "lat"), None, None),
            P("ord", "lat", None),
            P("lat"),
            P(),
            P("ord"),
            P(("lat", "ord"), None, None),
            P(),
            P(),
        ),
        out_specs=(P(("lat", "ord"), None, None), P(), P()),
        check_vma=False,
    )
```

```python
import math

import jax
import jax.numpy as jnp
from jax import lax
from jax.sharding import PartitionSpec as P


MESH_AXES = ("ord", "lat")
WRAP = 8


def device_of_block(k):
    n_ord, n_lat = lax.axis_size("ord"), lax.axis_size("lat")
    l, o = divmod(k, n_ord)
    return o * n_lat + l


def with_rims(field, width=2):
    count = lax.axis_size("ord") * lax.axis_size("lat")
    down_pairs = [(device_of_block(k), device_of_block(k + 1)) for k in range(count - 1)]
    up_pairs = [(device_of_block(k + 1), device_of_block(k)) for k in range(count - 1)]
    upper = lax.ppermute(field[field.shape[0] - width :], MESH_AXES, down_pairs)
    lower = lax.ppermute(field[:width], MESH_AXES, up_pairs)
    return jnp.concatenate([upper, field, lower], axis=0)


def group_sum(value, bits):
    count = lax.axis_size("ord") * lax.axis_size("lat")
    me = lax.axis_index("ord") * lax.axis_size("lat") + lax.axis_index("lat")
    size = 1 << len(bits)

    def mask_of(x):
        return sum(((x >> i) & 1) << bit for i, bit in enumerate(bits))

    held = [value]
    for x in range(1, size):
        mask = mask_of(x)
        held.append(lax.ppermute(value, MESH_AXES, [(d, d ^ mask) for d in range(count)]))
    held = jnp.stack(held)
    position = sum(((me >> bit) & 1) << i for i, bit in enumerate(bits))
    members = [lax.dynamic_index_in_dim(held, position ^ j, keepdims=False) for j in range(size)]
    while len(members) > 1:
        members = [members[i] + members[i + 1] for i in range(0, len(members), 2)]
    return members[0]


def butterfly_sum(value, carry, steps):
    count = lax.axis_size("ord") * lax.axis_size("lat")
    bits = list(range(count.bit_length() - 1))
    preferred = [(3, 4), (1, 2), (5, 6), (0,)]
    rounds = [tuple(b for b in group if b in bits) for group in preferred]
    rounds = [group for group in rounds if group]
    left = [b for b in bits if all(b not in group for group in rounds)]
    rounds += [(b,) for b in left]
    for round_index, group in enumerate(rounds):
        if round_index < len(steps):
            carry = steps[round_index](carry)
        value, carry = lax.optimization_barrier((group_sum(value, group), carry))
    for step in steps[len(rounds):]:
        carry = step(carry)
    return value, carry


def wrap_longitudes(field, width):
    return jnp.concatenate([field[:, -width:], field, field[:, :width]], axis=1)


def make_table(orders, length):
    lon_ids = jnp.arange(length, dtype=jnp.int32)
    residue = orders[:, None] * lon_ids[None, :] % length
    angles = residue.astype(jnp.float32) * (2.0 * math.pi / length)
    factor = jnp.where((orders == 0) | (2 * orders == length), 1.0, 2.0).astype(jnp.float32)[
        :, None
    ]
    parts = [factor * jnp.cos(angles), -factor * jnp.sin(angles)]
    return jnp.concatenate(parts, axis=1).astype(jnp.bfloat16)


def layer(
    grad_coef, legendre, quad_weight, slot_order, slot_count, conv_input, depth_kernel, point_weight
):
    n_ord = lax.axis_size("ord")
    n_lat = lax.axis_size("lat")
    own_slots, degrees, doubled = grad_coef.shape
    row_count, channels, longitudes = conv_input.shape
    lat_index = lax.axis_index("lat")

    x_rows = with_rims(conv_input.transpose(0, 2, 1))
    x_pad = wrap_longitudes(x_rows.astype(jnp.float32), WRAP)

    leg_rows = lax.all_to_all(legendre, "lat", 0, 1, tiled=True)
    spread = jnp.broadcast_to(quad_weight[None], (n_lat,) + quad_weight.shape)
    weights = lax.all_to_all(spread, "lat", 0, 0, tiled=True).reshape(-1)
    counts = lax.dynamic_slice_in_dim(slot_count, lat_index * own_slots, own_slots)
    is_valid = jnp.arange(degrees, dtype=jnp.int32)[None, :] < counts[:, None]
    masked = grad_coef * is_valid[:, :, None].astype(grad_coef.dtype)
    source = jnp.arange(doubled, dtype=jnp.int32)
    target = (source % 2) * channels + source // 2
    permute = (target[:, None] == source[None, :]).astype(grad_coef.dtype)
    masked = jnp.einsum("sjk,kt->sjt", masked, permute, preferred_element_type=jnp.float32)
    masked = masked.astype(grad_coef.dtype)
    summed = jnp.einsum("slj,sjk->slk", leg_rows, masked, preferred_element_type=jnp.float32)
    spectral = (summed * weights[None, :, None]).astype(jnp.bfloat16)
    by_device = spectral.reshape(own_slots, n_lat, n_ord, row_count * doubled)
    by_device = by_device.transpose(0, 2, 1, 3).reshape(own_slots, n_ord * n_lat, -1)
    own_rows = lax.all_to_all(by_device, MESH_AXES, 1, 0, tiled=True)
    own_rows = own_rows.reshape(-1, row_count * doubled)

    table = make_table(slot_order, longitudes)
    per_row = own_rows.reshape(-1, row_count, doubled)
    grid_rows = []
    for row in range(row_count):
        both = jnp.einsum("sq,sn->qn", table, per_row[:, row], preferred_element_type=jnp.float32)
        grid_rows.append(both[:longitudes, :channels] + both[longitudes:, channels:])
    grad_grid = jnp.stack(grid_rows).astype(jnp.bfloat16)

    hidden = jnp.zeros((row_count, longitudes, channels), jnp.float32)
    for tap_row in range(5):
        for tap_col in range(5):
            weight_tap = depth_kernel[:, 5 * tap_row + tap_col]
            start = WRAP - 2 + tap_col
            hidden = hidden + weight_tap * x_pad[
                tap_row : tap_row + row_count, start : start + longitudes
            ]
    hidden = hidden.astype(jnp.bfloat16)
    grad_hidden = jnp.einsum(
        "rqd,cd->rqc", grad_grid, point_weight, preferred_element_type=jnp.float32
    ).astype(jnp.bfloat16)
    point_part = jnp.einsum("rqc,rqd->cd", hidden, grad_grid, preferred_element_type=jnp.float32)
    hidden_wide = grad_hidden.astype(jnp.float32)
    depth_terms = []
    for tap_row in range(5):
        for tap_col in range(5):
            start = WRAP - 2 + tap_col
            shifted_x = x_pad[tap_row : tap_row + row_count, start : start + longitudes]
            depth_terms.append(jnp.sum(hidden_wide * shifted_x, axis=(0, 1)))
    depth_part = jnp.stack(depth_terms, axis=1)
    grad_pad = wrap_longitudes(with_rims(grad_hidden).astype(jnp.float32), WRAP)
    taps = [(tap_row, tap_col) for tap_row in range(5) for tap_col in range(5)]
    rounds = 4
    groups = [taps[i * len(taps) // rounds : (i + 1) * len(taps) // rounds] for i in range(rounds)]

    def tap_group(group):
        def step(grad_input):
            for tap_row, tap_col in group:
                weight_tap = depth_kernel[:, 5 * tap_row + tap_col]
                start = WRAP + 2 - tap_col
                grad_input = grad_input + weight_tap * grad_pad[
                    4 - tap_row : 4 - tap_row + row_count, start : start + longitudes
                ]
            return grad_input

        return step

    grad_input = jnp.zeros((row_count, longitudes, channels), jnp.float32)
    sums, grad_input = butterfly_sum(
        jnp.concatenate([point_part, depth_part], axis=1),
        grad_input,
        [tap_group(group) for group in groups],
    )
    grad_input = grad_input.astype(jnp.bfloat16).transpose(0, 2, 1)
    total_rows = row_count * n_ord * n_lat
    grad_scale = 1.0 / math.sqrt(total_rows * longitudes)
    sums = sums * grad_scale
    return (grad_input, sums[:, :channels], sums[:, channels:])


def solution(mesh):
    return jax.shard_map(
        layer,
        mesh=mesh,
        in_specs=(
            P(("ord", "lat"), None, None),
            P("ord", "lat", None),
            P("lat"),
            P(),
            P("ord"),
            P(("lat", "ord"), None, None),
            P(),
            P(),
        ),
        out_specs=(P(("lat", "ord"), None, None), P(), P()),
        check_vma=False,
    )
```

```python
import math

import jax
import jax.numpy as jnp
from jax import lax
from jax.sharding import PartitionSpec as P


MESH_AXES = ("ord", "lat")
WRAP = 8


def device_of_block(k):
    n_ord, n_lat = lax.axis_size("ord"), lax.axis_size("lat")
    l, o = divmod(k, n_ord)
    return o * n_lat + l


def with_rims(field, width=2):
    count = lax.axis_size("ord") * lax.axis_size("lat")
    down_pairs = [(device_of_block(k), device_of_block(k + 1)) for k in range(count - 1)]
    up_pairs = [(device_of_block(k + 1), device_of_block(k)) for k in range(count - 1)]
    upper = lax.ppermute(field[field.shape[0] - width :], MESH_AXES, down_pairs)
    lower = lax.ppermute(field[:width], MESH_AXES, up_pairs)
    return jnp.concatenate([upper, field, lower], axis=0)


def group_sum(value, bits):
    count = lax.axis_size("ord") * lax.axis_size("lat")
    me = lax.axis_index("ord") * lax.axis_size("lat") + lax.axis_index("lat")
    size = 1 << len(bits)

    def mask_of(x):
        return sum(((x >> i) & 1) << bit for i, bit in enumerate(bits))

    held = [value]
    for x in range(1, size):
        mask = mask_of(x)
        held.append(lax.ppermute(value, MESH_AXES, [(d, d ^ mask) for d in range(count)]))
    held = jnp.stack(held)
    position = sum(((me >> bit) & 1) << i for i, bit in enumerate(bits))
    members = [lax.dynamic_index_in_dim(held, position ^ j, keepdims=False) for j in range(size)]
    while len(members) > 1:
        members = [members[i] + members[i + 1] for i in range(0, len(members), 2)]
    return members[0]


def butterfly_sum(value, carry, steps):
    count = lax.axis_size("ord") * lax.axis_size("lat")
    bits = list(range(count.bit_length() - 1))
    preferred = [(3, 4), (1, 2), (5, 6), (0,)]
    rounds = [tuple(b for b in group if b in bits) for group in preferred]
    rounds = [group for group in rounds if group]
    left = [b for b in bits if all(b not in group for group in rounds)]
    rounds += [(b,) for b in left]
    for round_index, group in enumerate(rounds):
        if round_index < len(steps):
            carry = steps[round_index](carry)
        value, carry = lax.optimization_barrier((group_sum(value, group), carry))
    for step in steps[len(rounds):]:
        carry = step(carry)
    return value, carry


def lat_exchange(payload):
    count = lax.axis_size("lat")
    me = lax.axis_index("lat")
    pieces = []
    for shift in range(1, count):
        outgoing = lax.dynamic_index_in_dim(payload, (me + shift) % count, keepdims=False)
        pairs = [(i, (i + shift) % count) for i in range(count)]
        pieces.append(lax.ppermute(outgoing, "lat", pairs))
    own = lax.dynamic_index_in_dim(payload, me, keepdims=False)
    stacked = jnp.stack([own] + pieces)
    sources = (me - jnp.arange(count)) % count
    arranged = jnp.zeros_like(stacked).at[sources].set(stacked)
    return arranged


def wrap_longitudes(field, width):
    return jnp.concatenate([field[:, -width:], field, field[:, :width]], axis=1)


def make_table(orders, length):
    lon_ids = jnp.arange(length, dtype=jnp.int32)
    residue = orders[:, None] * lon_ids[None, :] % length
    angles = residue.astype(jnp.float32) * (2.0 * math.pi / length)
    factor = jnp.where((orders == 0) | (2 * orders == length), 1.0, 2.0).astype(jnp.float32)[
        :, None
    ]
    parts = [factor * jnp.cos(angles), -factor * jnp.sin(angles)]
    return jnp.concatenate(parts, axis=1).astype(jnp.bfloat16)


def layer(
    grad_coef, legendre, quad_weight, slot_order, slot_count, conv_input, depth_kernel, point_weight
):
    n_ord = lax.axis_size("ord")
    n_lat = lax.axis_size("lat")
    own_slots, degrees, doubled = grad_coef.shape
    row_count, channels, longitudes = conv_input.shape
    lat_index = lax.axis_index("lat")

    x_rows = with_rims(conv_input.transpose(0, 2, 1))
    x_pad = wrap_longitudes(x_rows.astype(jnp.float32), WRAP)

    _, band_rows, _ = legendre.shape
    pieces = []
    rest = quad_weight
    for _ in range(4):
        piece = lax.reduce_precision(rest, exponent_bits=8, mantissa_bits=7)
        pieces.append(piece.astype(jnp.bfloat16))
        rest = rest - piece
    extra = jnp.concatenate(pieces)
    extra = jnp.pad(extra, (0, degrees - extra.shape[0]))
    extra = jnp.broadcast_to(extra, (n_lat, 8, degrees))
    chunks = legendre.reshape(n_lat, own_slots * band_rows, degrees)
    payload = jnp.concatenate([chunks, extra.astype(legendre.dtype)], axis=1)
    arrived = lat_exchange(payload)
    body = arrived[:, : own_slots * band_rows].reshape(n_lat, own_slots, band_rows, degrees)
    leg_rows = body.transpose(1, 0, 2, 3).reshape(own_slots, n_lat * band_rows, degrees)
    parts = arrived[:, own_slots * band_rows, : 4 * band_rows].astype(jnp.float32)
    parts = parts.reshape(n_lat, 4, band_rows)
    weights = ((parts[:, 3] + parts[:, 2]) + parts[:, 1]) + parts[:, 0]
    weights = weights.reshape(-1)
    counts = lax.dynamic_slice_in_dim(slot_count, lat_index * own_slots, own_slots)
    is_valid = jnp.arange(degrees, dtype=jnp.int32)[None, :] < counts[:, None]
    masked = grad_coef * is_valid[:, :, None].astype(grad_coef.dtype)
    source = jnp.arange(doubled, dtype=jnp.int32)
    target = (source % 2) * channels + source // 2
    permute = (target[:, None] == source[None, :]).astype(grad_coef.dtype)
    masked = jnp.einsum("sjk,kt->sjt", masked, permute, preferred_element_type=jnp.float32)
    masked = masked.astype(grad_coef.dtype)
    summed = jnp.einsum("slj,sjk->slk", leg_rows, masked, preferred_element_type=jnp.float32)
    spectral = (summed * weights[None, :, None]).astype(jnp.bfloat16)
    by_device = spectral.reshape(own_slots, n_lat, n_ord, row_count * doubled)
    by_device = by_device.transpose(0, 2, 1, 3).reshape(own_slots, n_ord * n_lat, -1)
    own_rows = lax.all_to_all(by_device, MESH_AXES, 1, 0, tiled=True)
    own_rows = own_rows.reshape(-1, row_count * doubled)

    table = make_table(slot_order, longitudes)
    per_row = own_rows.reshape(-1, row_count, doubled)
    grid_rows = []
    for row in range(row_count):
        both = jnp.einsum("sq,sn->qn", table, per_row[:, row], preferred_element_type=jnp.float32)
        grid_rows.append(both[:longitudes, :channels] + both[longitudes:, channels:])
    grad_grid = jnp.stack(grid_rows).astype(jnp.bfloat16)

    hidden = jnp.zeros((row_count, longitudes, channels), jnp.float32)
    for tap_row in range(5):
        for tap_col in range(5):
            weight_tap = depth_kernel[:, 5 * tap_row + tap_col]
            start = WRAP - 2 + tap_col
            hidden = hidden + weight_tap * x_pad[
                tap_row : tap_row + row_count, start : start + longitudes
            ]
    hidden = hidden.astype(jnp.bfloat16)
    grad_hidden = jnp.einsum(
        "rqd,cd->rqc", grad_grid, point_weight, preferred_element_type=jnp.float32
    ).astype(jnp.bfloat16)
    point_part = jnp.einsum("rqc,rqd->cd", hidden, grad_grid, preferred_element_type=jnp.float32)
    hidden_wide = grad_hidden.astype(jnp.float32)
    depth_terms = []
    for tap_row in range(5):
        for tap_col in range(5):
            start = WRAP - 2 + tap_col
            shifted_x = x_pad[tap_row : tap_row + row_count, start : start + longitudes]
            depth_terms.append(jnp.sum(hidden_wide * shifted_x, axis=(0, 1)))
    depth_part = jnp.stack(depth_terms, axis=1)
    grad_pad = wrap_longitudes(with_rims(grad_hidden).astype(jnp.float32), WRAP)
    taps = [(tap_row, tap_col) for tap_row in range(5) for tap_col in range(5)]
    rounds = 4
    groups = [taps[i * len(taps) // rounds : (i + 1) * len(taps) // rounds] for i in range(rounds)]

    def tap_group(group):
        def step(grad_input):
            for tap_row, tap_col in group:
                weight_tap = depth_kernel[:, 5 * tap_row + tap_col]
                start = WRAP + 2 - tap_col
                grad_input = grad_input + weight_tap * grad_pad[
                    4 - tap_row : 4 - tap_row + row_count, start : start + longitudes
                ]
            return grad_input

        return step

    grad_input = jnp.zeros((row_count, longitudes, channels), jnp.float32)
    sums, grad_input = butterfly_sum(
        jnp.concatenate([point_part, depth_part], axis=1),
        grad_input,
        [tap_group(group) for group in groups],
    )
    grad_input = grad_input.astype(jnp.bfloat16).transpose(0, 2, 1)
    total_rows = row_count * n_ord * n_lat
    grad_scale = 1.0 / math.sqrt(total_rows * longitudes)
    sums = sums * grad_scale
    return (grad_input, sums[:, :channels], sums[:, channels:])


def solution(mesh):
    return jax.shard_map(
        layer,
        mesh=mesh,
        in_specs=(
            P(("ord", "lat"), None, None),
            P("ord", "lat", None),
            P("lat"),
            P(),
            P("ord"),
            P(("lat", "ord"), None, None),
            P(),
            P(),
        ),
        out_specs=(P(("lat", "ord"), None, None), P(), P()),
        check_vma=False,
    )
```

```python
import math

import jax
import jax.numpy as jnp
from jax import lax
from jax.sharding import PartitionSpec as P


MESH_AXES = ("ord", "lat")
WRAP = 8


def device_of_block(k):
    n_ord, n_lat = lax.axis_size("ord"), lax.axis_size("lat")
    l, o = divmod(k, n_ord)
    return o * n_lat + l


def with_rims(field, width=2):
    count = lax.axis_size("ord") * lax.axis_size("lat")
    down_pairs = [(device_of_block(k), device_of_block(k + 1)) for k in range(count - 1)]
    up_pairs = [(device_of_block(k + 1), device_of_block(k)) for k in range(count - 1)]
    upper = lax.ppermute(field[field.shape[0] - width :], MESH_AXES, down_pairs)
    lower = lax.ppermute(field[:width], MESH_AXES, up_pairs)
    return jnp.concatenate([upper, field, lower], axis=0)


def group_sum(value, bits):
    count = lax.axis_size("ord") * lax.axis_size("lat")
    me = lax.axis_index("ord") * lax.axis_size("lat") + lax.axis_index("lat")
    size = 1 << len(bits)

    def mask_of(x):
        return sum(((x >> i) & 1) << bit for i, bit in enumerate(bits))

    held = [value]
    for x in range(1, size):
        mask = mask_of(x)
        held.append(lax.ppermute(value, MESH_AXES, [(d, d ^ mask) for d in range(count)]))
    held = jnp.stack(held)
    position = sum(((me >> bit) & 1) << i for i, bit in enumerate(bits))
    members = [lax.dynamic_index_in_dim(held, position ^ j, keepdims=False) for j in range(size)]
    while len(members) > 1:
        members = [members[i] + members[i + 1] for i in range(0, len(members), 2)]
    return members[0]


def butterfly_sum(value, carry, steps):
    count = lax.axis_size("ord") * lax.axis_size("lat")
    bits = list(range(count.bit_length() - 1))
    preferred = [(3, 4), (1, 2), (5, 6), (0,)]
    rounds = [tuple(b for b in group if b in bits) for group in preferred]
    rounds = [group for group in rounds if group]
    left = [b for b in bits if all(b not in group for group in rounds)]
    rounds += [(b,) for b in left]
    for round_index, group in enumerate(rounds):
        if round_index < len(steps):
            carry = steps[round_index](carry)
        value, carry = lax.optimization_barrier((group_sum(value, group), carry))
    for step in steps[len(rounds):]:
        carry = step(carry)
    return value, carry


def wrap_longitudes(field, width):
    return jnp.concatenate([field[:, -width:], field, field[:, :width]], axis=1)


def make_table(orders, length):
    lon_ids = jnp.arange(length, dtype=jnp.int32)
    residue = orders[:, None] * lon_ids[None, :] % length
    angles = residue.astype(jnp.float32) * (2.0 * math.pi / length)
    factor = jnp.where((orders == 0) | (2 * orders == length), 1.0, 2.0).astype(jnp.float32)[
        :, None
    ]
    parts = [factor * jnp.cos(angles), -factor * jnp.sin(angles)]
    return jnp.concatenate(parts, axis=1).astype(jnp.bfloat16)


def layer(
    grad_coef, legendre, quad_weight, slot_order, slot_count, conv_input, depth_kernel, point_weight
):
    n_ord = lax.axis_size("ord")
    n_lat = lax.axis_size("lat")
    own_slots, degrees, doubled = grad_coef.shape
    row_count, channels, longitudes = conv_input.shape
    lat_index = lax.axis_index("lat")

    x_rows = with_rims(conv_input.transpose(0, 2, 1))
    x_pad = wrap_longitudes(x_rows.astype(jnp.float32), WRAP)

    _, band_rows, _ = legendre.shape
    pieces = []
    rest = quad_weight
    for _ in range(4):
        piece = lax.reduce_precision(rest, exponent_bits=8, mantissa_bits=7)
        pieces.append(piece.astype(jnp.bfloat16))
        rest = rest - piece
    extra = jnp.concatenate(pieces)
    extra = jnp.pad(extra, (0, degrees - extra.shape[0]))
    extra = jnp.broadcast_to(extra, (n_lat, 8, degrees))
    chunks = legendre.reshape(n_lat, own_slots * band_rows, degrees)
    payload = jnp.concatenate([chunks, extra.astype(legendre.dtype)], axis=1)
    arrived = lax.all_to_all(payload, "lat", 0, 0, tiled=True)
    body = arrived[:, : own_slots * band_rows].reshape(n_lat, own_slots, band_rows, degrees)
    leg_rows = body.transpose(1, 0, 2, 3).reshape(own_slots, n_lat * band_rows, degrees)
    parts = arrived[:, own_slots * band_rows, : 4 * band_rows].astype(jnp.float32)
    parts = parts.reshape(n_lat, 4, band_rows)
    weights = ((parts[:, 3] + parts[:, 2]) + parts[:, 1]) + parts[:, 0]
    weights = weights.reshape(-1)
    counts = lax.dynamic_slice_in_dim(slot_count, lat_index * own_slots, own_slots)
    is_valid = jnp.arange(degrees, dtype=jnp.int32)[None, :] < counts[:, None]
    masked = grad_coef * is_valid[:, :, None].astype(grad_coef.dtype)
    source = jnp.arange(doubled, dtype=jnp.int32)
    target = (source % 2) * channels + source // 2
    permute = (target[:, None] == source[None, :]).astype(grad_coef.dtype)
    masked = jnp.einsum("sjk,kt->sjt", masked, permute, preferred_element_type=jnp.float32)
    masked = masked.astype(grad_coef.dtype)
    summed = jnp.einsum("slj,sjk->slk", leg_rows, masked, preferred_element_type=jnp.float32)
    spectral = (summed * weights[None, :, None]).astype(jnp.bfloat16)
    by_device = spectral.reshape(own_slots, n_lat, n_ord, row_count * doubled)
    by_device = by_device.transpose(0, 2, 1, 3).reshape(own_slots, n_ord * n_lat, -1)
    own_rows = lax.all_to_all(by_device, MESH_AXES, 1, 0, tiled=True)
    own_rows = own_rows.reshape(-1, row_count * doubled)
    hidden = jnp.zeros((row_count, longitudes, channels), jnp.float32)
    for tap_row in range(5):
        for tap_col in range(5):
            weight_tap = depth_kernel[:, 5 * tap_row + tap_col]
            start = WRAP - 2 + tap_col
            hidden = hidden + weight_tap * x_pad[
                tap_row : tap_row + row_count, start : start + longitudes
            ]
    hidden = hidden.astype(jnp.bfloat16)
    own_rows, hidden = lax.optimization_barrier((own_rows, hidden))

    table = make_table(slot_order, longitudes)
    per_row = own_rows.reshape(-1, row_count, doubled)
    grid_rows = []
    for row in range(row_count):
        both = jnp.einsum("sq,sn->qn", table, per_row[:, row], preferred_element_type=jnp.float32)
        grid_rows.append(both[:longitudes, :channels] + both[longitudes:, channels:])
    grad_grid = jnp.stack(grid_rows).astype(jnp.bfloat16)

    grad_hidden = jnp.einsum(
        "rqd,cd->rqc", grad_grid, point_weight, preferred_element_type=jnp.float32
    ).astype(jnp.bfloat16)
    point_part = jnp.einsum("rqc,rqd->cd", hidden, grad_grid, preferred_element_type=jnp.float32)
    hidden_wide = grad_hidden.astype(jnp.float32)
    depth_terms = []
    for tap_row in range(5):
        for tap_col in range(5):
            start = WRAP - 2 + tap_col
            shifted_x = x_pad[tap_row : tap_row + row_count, start : start + longitudes]
            depth_terms.append(jnp.sum(hidden_wide * shifted_x, axis=(0, 1)))
    depth_part = jnp.stack(depth_terms, axis=1)
    grad_pad = wrap_longitudes(with_rims(grad_hidden).astype(jnp.float32), WRAP)
    taps = [(tap_row, tap_col) for tap_row in range(5) for tap_col in range(5)]
    rounds = 4
    groups = [taps[i * len(taps) // rounds : (i + 1) * len(taps) // rounds] for i in range(rounds)]

    def tap_group(group):
        def step(grad_input):
            for tap_row, tap_col in group:
                weight_tap = depth_kernel[:, 5 * tap_row + tap_col]
                start = WRAP + 2 - tap_col
                grad_input = grad_input + weight_tap * grad_pad[
                    4 - tap_row : 4 - tap_row + row_count, start : start + longitudes
                ]
            return grad_input

        return step

    grad_input = jnp.zeros((row_count, longitudes, channels), jnp.float32)
    sums, grad_input = butterfly_sum(
        jnp.concatenate([point_part, depth_part], axis=1),
        grad_input,
        [tap_group(group) for group in groups],
    )
    grad_input = grad_input.astype(jnp.bfloat16).transpose(0, 2, 1)
    total_rows = row_count * n_ord * n_lat
    grad_scale = 1.0 / math.sqrt(total_rows * longitudes)
    sums = sums * grad_scale
    return (grad_input, sums[:, :channels], sums[:, channels:])


def solution(mesh):
    return jax.shard_map(
        layer,
        mesh=mesh,
        in_specs=(
            P(("ord", "lat"), None, None),
            P("ord", "lat", None),
            P("lat"),
            P(),
            P("ord"),
            P(("lat", "ord"), None, None),
            P(),
            P(),
        ),
        out_specs=(P(("lat", "ord"), None, None), P(), P()),
        check_vma=False,
    )
```

```python
import math

import jax
import jax.numpy as jnp
from jax import lax
from jax.sharding import PartitionSpec as P


MESH_AXES = ("ord", "lat")
WRAP = 8


def device_of_block(k):
    n_ord, n_lat = lax.axis_size("ord"), lax.axis_size("lat")
    l, o = divmod(k, n_ord)
    return o * n_lat + l


def with_rims(field, width=2):
    count = lax.axis_size("ord") * lax.axis_size("lat")
    down_pairs = [(device_of_block(k), device_of_block(k + 1)) for k in range(count - 1)]
    up_pairs = [(device_of_block(k + 1), device_of_block(k)) for k in range(count - 1)]
    upper = lax.ppermute(field[field.shape[0] - width :], MESH_AXES, down_pairs)
    lower = lax.ppermute(field[:width], MESH_AXES, up_pairs)
    return jnp.concatenate([upper, field, lower], axis=0)


def group_sum(value, bits):
    count = lax.axis_size("ord") * lax.axis_size("lat")
    me = lax.axis_index("ord") * lax.axis_size("lat") + lax.axis_index("lat")
    size = 1 << len(bits)

    def mask_of(x):
        return sum(((x >> i) & 1) << bit for i, bit in enumerate(bits))

    held = [value]
    for x in range(1, size):
        mask = mask_of(x)
        held.append(lax.ppermute(value, MESH_AXES, [(d, d ^ mask) for d in range(count)]))
    held = jnp.stack(held)
    position = sum(((me >> bit) & 1) << i for i, bit in enumerate(bits))
    members = [lax.dynamic_index_in_dim(held, position ^ j, keepdims=False) for j in range(size)]
    while len(members) > 1:
        members = [members[i] + members[i + 1] for i in range(0, len(members), 2)]
    return members[0]


def butterfly_sum(value, carry, steps):
    count = lax.axis_size("ord") * lax.axis_size("lat")
    bits = list(range(count.bit_length() - 1))
    preferred = [(3, 4), (1, 2), (5, 6), (0,)]
    rounds = [tuple(b for b in group if b in bits) for group in preferred]
    rounds = [group for group in rounds if group]
    left = [b for b in bits if all(b not in group for group in rounds)]
    rounds += [(b,) for b in left]
    for round_index, group in enumerate(rounds):
        if round_index < len(steps):
            carry = steps[round_index](carry)
        value, carry = lax.optimization_barrier((group_sum(value, group), carry))
    for step in steps[len(rounds):]:
        carry = step(carry)
    return value, carry


def wrap_longitudes(field, width):
    return jnp.concatenate([field[:, -width:], field, field[:, :width]], axis=1)


def make_table(orders, length, outer):
    inner = length // outer
    step = 2.0 * math.pi / length
    m = orders[None, None, :]
    coarse = jnp.arange(outer, dtype=jnp.int32)[:, None, None]
    fine = jnp.arange(inner, dtype=jnp.int32)[None, :, None]
    angle_a = ((m * inner * coarse) % length).astype(jnp.float32) * step
    angle_b = ((m * fine) % length).astype(jnp.float32) * step
    cos_a, sin_a = jnp.cos(angle_a), jnp.sin(angle_a)
    cos_b, sin_b = jnp.cos(angle_b), jnp.sin(angle_b)
    cosine = cos_a * cos_b - sin_a * sin_b
    sine = sin_a * cos_b + cos_a * sin_b
    factor = jnp.where((orders == 0) | (2 * orders == length), 1.0, 2.0).astype(jnp.float32)
    parts = jnp.stack([factor * cosine, -factor * sine]).astype(jnp.bfloat16)
    return parts.reshape(2 * length, orders.shape[0])


def layer(
    grad_coef, legendre, quad_weight, slot_order, slot_count, conv_input, depth_kernel, point_weight
):
    n_ord = lax.axis_size("ord")
    n_lat = lax.axis_size("lat")
    own_slots, degrees, doubled = grad_coef.shape
    row_count, channels, longitudes = conv_input.shape
    lat_index = lax.axis_index("lat")

    x_rows = with_rims(conv_input.transpose(0, 2, 1))
    x_pad = wrap_longitudes(x_rows.astype(jnp.float32), WRAP)

    _, band_rows, _ = legendre.shape
    pieces = []
    rest = quad_weight
    for _ in range(4):
        piece = lax.reduce_precision(rest, exponent_bits=8, mantissa_bits=7)
        pieces.append(piece.astype(jnp.bfloat16))
        rest = rest - piece
    extra = jnp.concatenate(pieces)
    extra = jnp.pad(extra, (0, degrees - extra.shape[0]))
    extra = jnp.broadcast_to(extra, (n_lat, 8, degrees))
    chunks = legendre.reshape(n_lat, own_slots * band_rows, degrees)
    payload = jnp.concatenate([chunks, extra.astype(legendre.dtype)], axis=1)
    arrived = lax.all_to_all(payload, "lat", 0, 0, tiled=True)
    hidden = jnp.zeros((row_count, longitudes, channels), jnp.float32)
    for tap_row in range(5):
        for tap_col in range(5):
            weight_tap = depth_kernel[:, 5 * tap_row + tap_col]
            start = WRAP - 2 + tap_col
            hidden = hidden + weight_tap * x_pad[
                tap_row : tap_row + row_count, start : start + longitudes
            ]
    hidden = hidden.astype(jnp.bfloat16)
    counts = lax.dynamic_slice_in_dim(slot_count, lat_index * own_slots, own_slots)
    is_valid = jnp.arange(degrees, dtype=jnp.int32)[None, :] < counts[:, None]
    masked = grad_coef * is_valid[:, :, None].astype(grad_coef.dtype)
    source = jnp.arange(doubled, dtype=jnp.int32)
    target = (source % 2) * channels + source // 2
    permute = (target[:, None] == source[None, :]).astype(grad_coef.dtype)
    masked = jnp.einsum("sjk,kt->sjt", masked, permute, preferred_element_type=jnp.float32)
    masked = masked.astype(grad_coef.dtype)
    arrived, hidden, masked = lax.optimization_barrier((arrived, hidden, masked))
    body = arrived[:, : own_slots * band_rows].reshape(n_lat, own_slots, band_rows, degrees)
    leg_rows = body.transpose(1, 0, 2, 3).reshape(own_slots, n_lat * band_rows, degrees)
    parts = arrived[:, own_slots * band_rows, : 4 * band_rows].astype(jnp.float32)
    parts = parts.reshape(n_lat, 4, band_rows)
    weights = ((parts[:, 3] + parts[:, 2]) + parts[:, 1]) + parts[:, 0]
    weights = weights.reshape(-1)
    summed = jnp.einsum("slj,sjk->slk", leg_rows, masked, preferred_element_type=jnp.float32)
    spectral = (summed * weights[None, :, None]).astype(jnp.bfloat16)
    by_device = spectral.reshape(own_slots, n_lat, n_ord, row_count * doubled)
    by_device = by_device.transpose(0, 2, 1, 3).reshape(own_slots, n_ord * n_lat, -1)
    own_rows = lax.all_to_all(by_device, MESH_AXES, 1, 0, tiled=True)
    own_rows = own_rows.reshape(-1, row_count * doubled)

    table = make_table(slot_order, longitudes, 36 if longitudes % 36 == 0 else 1)
    per_row = own_rows.reshape(-1, row_count, doubled)
    grid_rows = []
    for row in range(row_count):
        both = jnp.einsum("qs,sn->qn", table, per_row[:, row], preferred_element_type=jnp.float32)
        grid_rows.append(both[:longitudes, :channels] + both[longitudes:, channels:])
    grad_grid = jnp.stack(grid_rows).astype(jnp.bfloat16)

    grad_hidden = jnp.einsum(
        "rqd,cd->rqc", grad_grid, point_weight, preferred_element_type=jnp.float32
    ).astype(jnp.bfloat16)
    point_part = jnp.einsum("rqc,rqd->cd", hidden, grad_grid, preferred_element_type=jnp.float32)
    hidden_wide = grad_hidden.astype(jnp.float32)
    depth_terms = []
    for tap_row in range(5):
        for tap_col in range(5):
            start = WRAP - 2 + tap_col
            shifted_x = x_pad[tap_row : tap_row + row_count, start : start + longitudes]
            depth_terms.append(jnp.sum(hidden_wide * shifted_x, axis=(0, 1)))
    depth_part = jnp.stack(depth_terms, axis=1)
    grad_pad = wrap_longitudes(with_rims(grad_hidden).astype(jnp.float32), WRAP)
    taps = [(tap_row, tap_col) for tap_row in range(5) for tap_col in range(5)]
    rounds = 4
    groups = [taps[i * len(taps) // rounds : (i + 1) * len(taps) // rounds] for i in range(rounds)]

    def tap_group(group):
        def step(grad_input):
            for tap_row, tap_col in group:
                weight_tap = depth_kernel[:, 5 * tap_row + tap_col]
                start = WRAP + 2 - tap_col
                grad_input = grad_input + weight_tap * grad_pad[
                    4 - tap_row : 4 - tap_row + row_count, start : start + longitudes
                ]
            return grad_input

        return step

    grad_input = jnp.zeros((row_count, longitudes, channels), jnp.float32)
    sums, grad_input = butterfly_sum(
        jnp.concatenate([point_part, depth_part], axis=1),
        grad_input,
        [tap_group(group) for group in groups],
    )
    grad_input = grad_input.astype(jnp.bfloat16).transpose(0, 2, 1)
    total_rows = row_count * n_ord * n_lat
    grad_scale = 1.0 / math.sqrt(total_rows * longitudes)
    sums = sums * grad_scale
    return (grad_input, sums[:, :channels], sums[:, channels:])


def solution(mesh):
    return jax.shard_map(
        layer,
        mesh=mesh,
        in_specs=(
            P(("ord", "lat"), None, None),
            P("ord", "lat", None),
            P("lat"),
            P(),
            P("ord"),
            P(("lat", "ord"), None, None),
            P(),
            P(),
        ),
        out_specs=(P(("lat", "ord"), None, None), P(), P()),
        check_vma=False,
    )
```

```python
import math

import jax
import jax.numpy as jnp
from jax import lax
from jax.sharding import PartitionSpec as P


MESH_AXES = ("ord", "lat")
WRAP = 8


def device_of_block(k):
    n_ord, n_lat = lax.axis_size("ord"), lax.axis_size("lat")
    l, o = divmod(k, n_ord)
    return o * n_lat + l


def with_rims(field, width=2):
    count = lax.axis_size("ord") * lax.axis_size("lat")
    down_pairs = [(device_of_block(k), device_of_block(k + 1)) for k in range(count - 1)]
    up_pairs = [(device_of_block(k + 1), device_of_block(k)) for k in range(count - 1)]
    upper = lax.ppermute(field[field.shape[0] - width :], MESH_AXES, down_pairs)
    lower = lax.ppermute(field[:width], MESH_AXES, up_pairs)
    return jnp.concatenate([upper, field, lower], axis=0)


def group_sum(value, bits):
    count = lax.axis_size("ord") * lax.axis_size("lat")
    me = lax.axis_index("ord") * lax.axis_size("lat") + lax.axis_index("lat")
    size = 1 << len(bits)

    def mask_of(x):
        return sum(((x >> i) & 1) << bit for i, bit in enumerate(bits))

    held = [value]
    for x in range(1, size):
        mask = mask_of(x)
        held.append(lax.ppermute(value, MESH_AXES, [(d, d ^ mask) for d in range(count)]))
    position = sum(((me >> bit) & 1) << i for i, bit in enumerate(bits))

    def member(j):
        chosen = held[size - 1]
        for x in range(size - 2, -1, -1):
            chosen = jnp.where((position ^ j) == x, held[x], chosen)
        return chosen

    members = [member(j) for j in range(size)]
    while len(members) > 1:
        members = [members[i] + members[i + 1] for i in range(0, len(members), 2)]
    return members[0]


def butterfly_sum(value, carry, steps):
    count = lax.axis_size("ord") * lax.axis_size("lat")
    bits = list(range(count.bit_length() - 1))
    preferred = [(3, 4), (1, 2), (5, 6), (0,)]
    rounds = [tuple(b for b in group if b in bits) for group in preferred]
    rounds = [group for group in rounds if group]
    left = [b for b in bits if all(b not in group for group in rounds)]
    rounds += [(b,) for b in left]
    for round_index, group in enumerate(rounds):
        if round_index < len(steps):
            carry = steps[round_index](carry)
        value, carry = lax.optimization_barrier((group_sum(value, group), carry))
    for step in steps[len(rounds):]:
        carry = step(carry)
    return value, carry


def wrap_longitudes(field, width):
    return jnp.concatenate([field[:, -width:], field, field[:, :width]], axis=1)


def make_table(orders, length, outer):
    inner = length // outer
    step = 2.0 * math.pi / length
    m = orders[None, None, :]
    coarse = jnp.arange(outer, dtype=jnp.int32)[:, None, None]
    fine = jnp.arange(inner, dtype=jnp.int32)[None, :, None]
    angle_a = ((m * inner * coarse) % length).astype(jnp.float32) * step
    angle_b = ((m * fine) % length).astype(jnp.float32) * step
    cos_a, sin_a = jnp.cos(angle_a), jnp.sin(angle_a)
    cos_b, sin_b = jnp.cos(angle_b), jnp.sin(angle_b)
    cosine = cos_a * cos_b - sin_a * sin_b
    sine = sin_a * cos_b + cos_a * sin_b
    factor = jnp.where((orders == 0) | (2 * orders == length), 1.0, 2.0).astype(jnp.float32)
    parts = jnp.stack([factor * cosine, -factor * sine]).astype(jnp.bfloat16)
    return parts.reshape(2 * length, orders.shape[0])


def layer(
    grad_coef, legendre, quad_weight, slot_order, slot_count, conv_input, depth_kernel, point_weight
):
    n_ord = lax.axis_size("ord")
    n_lat = lax.axis_size("lat")
    own_slots, degrees, doubled = grad_coef.shape
    row_count, channels, longitudes = conv_input.shape
    lat_index = lax.axis_index("lat")

    x_rows = with_rims(conv_input.transpose(0, 2, 1))
    x_pad = wrap_longitudes(x_rows.astype(jnp.float32), WRAP)

    _, band_rows, _ = legendre.shape
    pieces = []
    rest = quad_weight
    for _ in range(4):
        piece = lax.reduce_precision(rest, exponent_bits=8, mantissa_bits=7)
        pieces.append(piece.astype(jnp.bfloat16))
        rest = rest - piece
    extra = jnp.concatenate(pieces)
    extra = jnp.pad(extra, (0, degrees - extra.shape[0]))
    extra = jnp.broadcast_to(extra, (n_lat, 8, degrees))
    chunks = legendre.reshape(n_lat, own_slots * band_rows, degrees)
    payload = jnp.concatenate([chunks, extra.astype(legendre.dtype)], axis=1)
    arrived = lax.all_to_all(payload, "lat", 0, 0, tiled=True)
    hidden = jnp.zeros((row_count, longitudes, channels), jnp.float32)
    for tap_row in range(5):
        for tap_col in range(5):
            weight_tap = depth_kernel[:, 5 * tap_row + tap_col]
            start = WRAP - 2 + tap_col
            hidden = hidden + weight_tap * x_pad[
                tap_row : tap_row + row_count, start : start + longitudes
            ]
    hidden = hidden.astype(jnp.bfloat16)
    counts = lax.dynamic_slice_in_dim(slot_count, lat_index * own_slots, own_slots)
    is_valid = jnp.arange(degrees, dtype=jnp.int32)[None, :] < counts[:, None]
    masked = grad_coef * is_valid[:, :, None].astype(grad_coef.dtype)
    source = jnp.arange(doubled, dtype=jnp.int32)
    target = (source % 2) * channels + source // 2
    permute = (target[:, None] == source[None, :]).astype(grad_coef.dtype)
    masked = jnp.einsum("sjk,kt->sjt", masked, permute, preferred_element_type=jnp.float32)
    masked = masked.astype(grad_coef.dtype)
    arrived, hidden, masked = lax.optimization_barrier((arrived, hidden, masked))
    body = arrived[:, : own_slots * band_rows].reshape(n_lat, own_slots, band_rows, degrees)
    parts = arrived[:, own_slots * band_rows, : 4 * band_rows].astype(jnp.float32)
    parts = parts.reshape(n_lat, 4, band_rows)
    weights = ((parts[:, 3] + parts[:, 2]) + parts[:, 1]) + parts[:, 0]
    weights = weights.reshape(-1)
    summed = jnp.einsum("lsrj,sjk->slrk", body, masked, preferred_element_type=jnp.float32)
    summed = summed.reshape(own_slots, n_lat * band_rows, doubled)
    spectral = (summed * weights[None, :, None]).astype(jnp.bfloat16)
    by_device = spectral.reshape(own_slots, n_lat, n_ord, row_count * doubled)
    by_device = by_device.transpose(0, 2, 1, 3).reshape(own_slots, n_ord * n_lat, -1)
    own_rows = lax.all_to_all(by_device, MESH_AXES, 1, 0, tiled=True)
    own_rows = own_rows.reshape(-1, row_count * doubled)

    table = make_table(slot_order, longitudes, 36 if longitudes % 36 == 0 else 1)
    per_row = own_rows.reshape(-1, row_count, doubled)
    grid_rows = []
    for row in range(row_count):
        both = jnp.einsum("qs,sn->qn", table, per_row[:, row], preferred_element_type=jnp.float32)
        grid_rows.append(both[:longitudes, :channels] + both[longitudes:, channels:])
    grad_grid = jnp.stack(grid_rows).astype(jnp.bfloat16)

    grad_hidden = jnp.einsum(
        "rqd,cd->rqc", grad_grid, point_weight, preferred_element_type=jnp.float32
    ).astype(jnp.bfloat16)
    point_part = jnp.einsum("rqc,rqd->cd", hidden, grad_grid, preferred_element_type=jnp.float32)
    hidden_wide = grad_hidden.astype(jnp.float32)
    depth_terms = []
    for tap_row in range(5):
        for tap_col in range(5):
            start = WRAP - 2 + tap_col
            shifted_x = x_pad[tap_row : tap_row + row_count, start : start + longitudes]
            depth_terms.append(jnp.sum(hidden_wide * shifted_x, axis=(0, 1)))
    depth_part = jnp.stack(depth_terms, axis=1)
    grad_pad = wrap_longitudes(with_rims(grad_hidden).astype(jnp.float32), WRAP)
    taps = [(tap_row, tap_col) for tap_row in range(5) for tap_col in range(5)]
    rounds = 4
    groups = [taps[i * len(taps) // rounds : (i + 1) * len(taps) // rounds] for i in range(rounds)]

    def tap_group(group):
        def step(grad_input):
            for tap_row, tap_col in group:
                weight_tap = depth_kernel[:, 5 * tap_row + tap_col]
                start = WRAP + 2 - tap_col
                grad_input = grad_input + weight_tap * grad_pad[
                    4 - tap_row : 4 - tap_row + row_count, start : start + longitudes
                ]
            return grad_input

        return step

    grad_input = jnp.zeros((row_count, longitudes, channels), jnp.float32)
    sums, grad_input = butterfly_sum(
        jnp.concatenate([point_part, depth_part], axis=1),
        grad_input,
        [tap_group(group) for group in groups],
    )
    grad_input = grad_input.astype(jnp.bfloat16).transpose(0, 2, 1)
    total_rows = row_count * n_ord * n_lat
    grad_scale = 1.0 / math.sqrt(total_rows * longitudes)
    sums = sums * grad_scale
    return (grad_input, sums[:, :channels], sums[:, channels:])


def solution(mesh):
    return jax.shard_map(
        layer,
        mesh=mesh,
        in_specs=(
            P(("ord", "lat"), None, None),
            P("ord", "lat", None),
            P("lat"),
            P(),
            P("ord"),
            P(("lat", "ord"), None, None),
            P(),
            P(),
        ),
        out_specs=(P(("lat", "ord"), None, None), P(), P()),
        check_vma=False,
    )
```

```python
import math

import jax
import jax.numpy as jnp
from jax import lax
from jax.sharding import PartitionSpec as P


MESH_AXES = ("ord", "lat")
WRAP = 8


def device_of_block(k):
    n_ord, n_lat = lax.axis_size("ord"), lax.axis_size("lat")
    l, o = divmod(k, n_ord)
    return o * n_lat + l


def with_rims(field, width=2):
    count = lax.axis_size("ord") * lax.axis_size("lat")
    down_pairs = [(device_of_block(k), device_of_block(k + 1)) for k in range(count - 1)]
    up_pairs = [(device_of_block(k + 1), device_of_block(k)) for k in range(count - 1)]
    upper = lax.ppermute(field[field.shape[0] - width :], MESH_AXES, down_pairs)
    lower = lax.ppermute(field[:width], MESH_AXES, up_pairs)
    return jnp.concatenate([upper, field, lower], axis=0)


def group_sum(value, bits):
    count = lax.axis_size("ord") * lax.axis_size("lat")
    me = lax.axis_index("ord") * lax.axis_size("lat") + lax.axis_index("lat")
    size = 1 << len(bits)

    def mask_of(x):
        return sum(((x >> i) & 1) << bit for i, bit in enumerate(bits))

    held = [value]
    for x in range(1, size):
        mask = mask_of(x)
        held.append(lax.ppermute(value, MESH_AXES, [(d, d ^ mask) for d in range(count)]))
    position = sum(((me >> bit) & 1) << i for i, bit in enumerate(bits))

    def member(j):
        chosen = held[size - 1]
        for x in range(size - 2, -1, -1):
            chosen = jnp.where((position ^ j) == x, held[x], chosen)
        return chosen

    members = [member(j) for j in range(size)]
    while len(members) > 1:
        members = [members[i] + members[i + 1] for i in range(0, len(members), 2)]
    return members[0]


def butterfly_sum(value, carry, steps):
    count = lax.axis_size("ord") * lax.axis_size("lat")
    bits = list(range(count.bit_length() - 1))
    preferred = [(3, 4), (1, 2), (5, 6), (0,)]
    rounds = [tuple(b for b in group if b in bits) for group in preferred]
    rounds = [group for group in rounds if group]
    left = [b for b in bits if all(b not in group for group in rounds)]
    rounds += [(b,) for b in left]
    for round_index, group in enumerate(rounds):
        if round_index < len(steps):
            carry = steps[round_index](carry)
        value, carry = lax.optimization_barrier((group_sum(value, group), carry))
    for step in steps[len(rounds):]:
        carry = step(carry)
    return value, carry


def wrap_longitudes(field, width):
    return jnp.concatenate([field[:, -width:], field, field[:, :width]], axis=1)


def make_table(orders, length, outer):
    inner = length // outer
    step = 2.0 * math.pi / length
    m = orders[None, None, :]
    coarse = jnp.arange(outer, dtype=jnp.int32)[:, None, None]
    fine = jnp.arange(inner, dtype=jnp.int32)[None, :, None]
    angle_a = ((m * inner * coarse) % length).astype(jnp.float32) * step
    angle_b = ((m * fine) % length).astype(jnp.float32) * step
    cos_a, sin_a = jnp.cos(angle_a), jnp.sin(angle_a)
    cos_b, sin_b = jnp.cos(angle_b), jnp.sin(angle_b)
    cosine = cos_a * cos_b - sin_a * sin_b
    sine = sin_a * cos_b + cos_a * sin_b
    factor = jnp.where((orders == 0) | (2 * orders == length), 1.0, 2.0).astype(jnp.float32)
    parts = jnp.stack([factor * cosine, -factor * sine]).astype(jnp.bfloat16)
    return parts.reshape(2 * length, orders.shape[0])


def layer(
    grad_coef, legendre, quad_weight, slot_order, slot_count, conv_input, depth_kernel, point_weight
):
    n_ord = lax.axis_size("ord")
    n_lat = lax.axis_size("lat")
    own_slots, degrees, doubled = grad_coef.shape
    row_count, channels, longitudes = conv_input.shape
    lat_index = lax.axis_index("lat")

    x_rows = with_rims(conv_input.transpose(0, 2, 1))
    x_pad = wrap_longitudes(x_rows.astype(jnp.float32), WRAP)

    _, band_rows, _ = legendre.shape
    pieces = []
    rest = quad_weight
    for _ in range(4):
        piece = lax.reduce_precision(rest, exponent_bits=8, mantissa_bits=7)
        pieces.append(piece.astype(jnp.bfloat16))
        rest = rest - piece
    extra = jnp.concatenate(pieces)
    extra = jnp.pad(extra, (0, degrees - extra.shape[0]))
    extra = jnp.broadcast_to(extra, (n_lat, 8, degrees))
    chunks = legendre.reshape(n_lat, own_slots * band_rows, degrees)
    payload = jnp.concatenate([chunks, extra.astype(legendre.dtype)], axis=1)
    arrived = lax.all_to_all(payload, "lat", 0, 0, tiled=True)
    hidden = jnp.zeros((row_count, longitudes, channels), jnp.float32)
    for tap_row in range(5):
        for tap_col in range(5):
            weight_tap = depth_kernel[:, 5 * tap_row + tap_col]
            start = WRAP - 2 + tap_col
            hidden = hidden + weight_tap * x_pad[
                tap_row : tap_row + row_count, start : start + longitudes
            ]
    hidden = hidden.astype(jnp.bfloat16)
    counts = lax.dynamic_slice_in_dim(slot_count, lat_index * own_slots, own_slots)
    is_valid = jnp.arange(degrees, dtype=jnp.int32)[None, :] < counts[:, None]
    masked = grad_coef * is_valid[:, :, None].astype(grad_coef.dtype)
    source = jnp.arange(doubled, dtype=jnp.int32)
    target = (source % 2) * channels + source // 2
    permute = (target[:, None] == source[None, :]).astype(grad_coef.dtype)
    masked = jnp.einsum("sjk,kt->sjt", masked, permute, preferred_element_type=jnp.float32)
    masked = masked.astype(grad_coef.dtype)
    arrived, hidden, masked = lax.optimization_barrier((arrived, hidden, masked))
    body = arrived[:, : own_slots * band_rows].reshape(n_lat, own_slots, band_rows, degrees)
    leg_rows = body.transpose(1, 0, 2, 3).reshape(own_slots, n_lat * band_rows, degrees)
    parts = arrived[:, own_slots * band_rows, : 4 * band_rows].astype(jnp.float32)
    parts = parts.reshape(n_lat, 4, band_rows)
    weights = ((parts[:, 3] + parts[:, 2]) + parts[:, 1]) + parts[:, 0]
    weights = weights.reshape(-1)
    summed = jnp.einsum("slj,sjk->slk", leg_rows, masked, preferred_element_type=jnp.float32)
    spectral = (summed * weights[None, :, None]).astype(jnp.bfloat16)
    by_device = spectral.reshape(own_slots, n_lat, n_ord, row_count * doubled)
    by_device = by_device.transpose(0, 2, 1, 3).reshape(own_slots, n_ord * n_lat, -1)
    own_rows = lax.all_to_all(by_device, MESH_AXES, 1, 0, tiled=True)
    own_rows = own_rows.reshape(-1, row_count * doubled)

    table = make_table(slot_order, longitudes, 36 if longitudes % 36 == 0 else 1)
    per_row = own_rows.reshape(-1, row_count, doubled)
    grid_rows = []
    for row in range(row_count):
        both = jnp.einsum("qs,sn->qn", table, per_row[:, row], preferred_element_type=jnp.float32)
        grid_rows.append(both[:longitudes, :channels] + both[longitudes:, channels:])
    grad_grid = jnp.stack(grid_rows).astype(jnp.bfloat16)

    grad_hidden = jnp.einsum(
        "rqd,cd->rqc", grad_grid, point_weight, preferred_element_type=jnp.float32
    ).astype(jnp.bfloat16)
    point_part = jnp.einsum("rqc,rqd->cd", hidden, grad_grid, preferred_element_type=jnp.float32)
    hidden_wide = grad_hidden.astype(jnp.float32)
    depth_terms = []
    for tap_row in range(5):
        for tap_col in range(5):
            start = WRAP - 2 + tap_col
            shifted_x = x_pad[tap_row : tap_row + row_count, start : start + longitudes]
            depth_terms.append(jnp.sum(hidden_wide * shifted_x, axis=(0, 1)))
    depth_part = jnp.stack(depth_terms, axis=1)
    grad_pad = wrap_longitudes(with_rims(grad_hidden).astype(jnp.float32), WRAP)
    taps = [(tap_row, tap_col) for tap_row in range(5) for tap_col in range(5)]
    rounds = 3
    groups = [taps[i * len(taps) // rounds : (i + 1) * len(taps) // rounds] for i in range(rounds)]

    def tap_group(group):
        def step(grad_input):
            for tap_row, tap_col in group:
                weight_tap = depth_kernel[:, 5 * tap_row + tap_col]
                start = WRAP + 2 - tap_col
                grad_input = grad_input + weight_tap * grad_pad[
                    4 - tap_row : 4 - tap_row + row_count, start : start + longitudes
                ]
            return grad_input

        return step

    def finish(grad_input):
        return grad_input.astype(jnp.bfloat16).transpose(0, 2, 1)

    grad_input = jnp.zeros((row_count, longitudes, channels), jnp.float32)
    sums, grad_input = butterfly_sum(
        jnp.concatenate([point_part, depth_part], axis=1),
        grad_input,
        [tap_group(group) for group in groups] + [finish],
    )
    total_rows = row_count * n_ord * n_lat
    grad_scale = 1.0 / math.sqrt(total_rows * longitudes)
    sums = sums * grad_scale
    return (grad_input, sums[:, :channels], sums[:, channels:])


def solution(mesh):
    return jax.shard_map(
        layer,
        mesh=mesh,
        in_specs=(
            P(("ord", "lat"), None, None),
            P("ord", "lat", None),
            P("lat"),
            P(),
            P("ord"),
            P(("lat", "ord"), None, None),
            P(),
            P(),
        ),
        out_specs=(P(("lat", "ord"), None, None), P(), P()),
        check_vma=False,
    )
```
